256 devices in a mesh: wide: 32 (over x, z), narrow: 8 (over y, core).
Axes of the slice: x: 4, y: 4, z: 8, core: 2. Of those that a mesh axis runs over, the one named last changes fastest.
Arguments:
- tensor: bfloat16 [256, 3, 1024, 1024], P('wide', None, 'narrow'), may hold values from -6 to 6
- occupied: bfloat16 [256, 3, 1024], replicated, may hold values from -0.625 to 0.625
- virtual: bfloat16 [256, 3, 1024], replicated, may hold values from -0.0007324219 to 0.0007324219
- atom_size: int32 [256], replicated, may hold values from 14 to 32, as said below
- tensor_pattern: int32 [256, 3], replicated, may hold values 0 or 1
- occupied_pattern: int32 [256, 3], replicated, may hold values 0 or 1
- virtual_pattern: int32 [256, 3], replicated, may hold values 0 or 1
Outputs:
- response: float32 [1024, 1024], P('wide', 'narrow')
The draws below stay inside these ranges and needn't reach their ends.
Inputs may be any that keep to these rules, and one draw needn't show every extreme that they name: Orbitals of an atom at and beyond its atom_size are padding.
All inputs are finite; a program needn't handle non-finite values.
Results may differ from the reference program's by a relative error of at most 0.0041.
Values may be sent and summed in bfloat16 or wider, within the bound.
No kernel may reach another device: no remote copies, remote signals or barrier semaphores. Data moves between devices by JAX's collectives and lax.ppermute only.
A program may use at most 192 MiB of HBM per device.

```python
import jax
import jax.numpy as jnp
from jax import lax

BO = 32
NBAND = 3
PCH = 1024
NA = 256


def draw_atom_size(key, part):
    first_key, second_key = jax.random.split(key)
    lowest = BO * 7 // 16
    counts = jax.random.randint(first_key, (NA,), lowest, BO + 1, dtype=jnp.int32)
    order = jax.random.permutation(second_key, NA)
    counts = counts.at[order[0]].set(BO).at[order[1]].set(lowest)
    return counts


def with_ends(entries, own_key, smallest, high):
    longest = entries.shape.index(max(entries.shape))
    spots = []
    for shift in (0, 1):
        where = [jax.random.randint(jax.random.fold_in(own_key, axis), (), 0, length) for axis, length in enumerate(entries.shape)]
        where[longest] = (where[longest] + shift) % entries.shape[longest]
        spots.append(tuple(where))
    return entries.at[spots[0]].set(smallest).at[spots[1]].set(high)


def with_spikes(result, own_key, source, target, shards_of, factor):
    owner, partner = [(jnp.arange(result.shape[dim]) // (result.shape[dim] // shards_of)).reshape([-1 if axis == dim else 1 for axis in range(result.ndim)]) for dim in (source, target)]
    chosen = jax.random.permutation(own_key, shards_of)[partner]
    strong = (owner == chosen) | (owner == (partner + shards_of // 2) % shards_of)
    return jnp.where(strong, factor * result, result)


def block_levels(key, dims, cuts, low, top_value):
    def one(dim, parts):
        draws = jax.random.uniform(jax.random.fold_in(jax.random.fold_in(key, 6), dim), (parts,), jnp.float32, low / len(cuts), top_value / len(cuts))
        return jnp.repeat(jnp.exp(draws), dims[dim] // parts).reshape((-1,) + (1,) * (len(dims) - dim - 1))

    level = one(*cuts[0])
    for cut in cuts[1:]:
        level = level * one(*cut)
    return level


def normal_values(key, shape, deviation, reach, cuts=(), kind=jnp.bfloat16):
    drawn = deviation * jax.random.normal(key, shape, jnp.float32)
    if cuts:
        drawn = drawn * block_levels(key, shape, cuts, -0.22, 0.18)
    return jnp.clip(drawn, -reach, reach).astype(kind)


def noise_with(rng, dims, spread, limit, pieces, heavy, kind=jnp.bfloat16):
    result = spread * jax.random.normal(rng, dims, jnp.float32)
    if pieces:
        result = result * block_levels(rng, dims, pieces, -0.22, 0.18)
    return jnp.clip(with_spikes(result, jax.random.fold_in(rng, 3), *heavy), -limit, limit).astype(kind)


def setup_inputs(seed: int = 0) -> dict:
    key_of = jax.random.split(jax.random.key(seed), 8)
    return {
        "tensor": noise_with(key_of[0], (NA, NBAND, PCH, BO * BO), 1.0, 6.0, ((0, 32), (2, 8)), (0, 2, 32, 2.75)),
        "occupied": normal_values(key_of[1], (NA, NBAND, BO * BO), (NBAND * BO) ** -0.5, 0.625),
        "virtual": normal_values(key_of[2], (NA, NBAND, BO * BO), (NBAND * BO * NA * 5 * BO * BO // 2) ** -0.5, 0.0007324219),
        "atom_size": draw_atom_size(jax.random.fold_in(key_of[7], 71), 0),
        "tensor_pattern": with_ends((jax.random.randint(key_of[4], (NA, NBAND), 0, 4) < 3).astype(jnp.int32), jax.random.fold_in(key_of[4], 1), 0, 1),
        "occupied_pattern": with_ends((jax.random.randint(key_of[5], (NA, NBAND), 0, 4) < 3).astype(jnp.int32), jax.random.fold_in(key_of[5], 1), 0, 1),
        "virtual_pattern": with_ends((jax.random.randint(key_of[6], (NA, NBAND), 0, 4) < 3).astype(jnp.int32), jax.random.fold_in(key_of[6], 1), 0, 1),
    }


def block_masks(size_pad, tensor_flags, occupied_flags, virtual_flags, atom_index):
    nearby_sizes = lax.dynamic_slice(size_pad, (atom_index,), (5,))
    present = (nearby_sizes > 0).astype(jnp.int32)
    orbital = jnp.arange(BO, dtype=jnp.int32)
    zero_index = jnp.zeros((), jnp.int32)
    row_flags = lax.dynamic_slice(tensor_flags, (atom_index + 1, zero_index), (3, 3))
    row_ok = (orbital[None, :] < nearby_sizes[1:4, None]).astype(jnp.int32)
    partner = jnp.stack([nearby_sizes[r:r + 3] for r in range(3)])
    column_ok = (orbital[None, None, :] < partner[:, :, None]).astype(jnp.int32)
    entry_mask = row_flags[:, :, None, None] * row_ok[:, None, :, None] * column_ok[:, :, None, :]
    tensor_mask = entry_mask.reshape(3, 3, 1, BO * BO).astype(jnp.bfloat16)
    occupied_mask = lax.dynamic_slice(occupied_flags, (atom_index + 2, zero_index), (1, 3))[0] * present[1:4]
    partner_present = jnp.stack([present[r:r + 3] for r in range(3)])
    virtual_mask = lax.dynamic_slice(virtual_flags, (atom_index + 1, zero_index), (3, 3)) * present[1:4, None] * partner_present
    return tensor_mask, occupied_mask.astype(jnp.bfloat16), virtual_mask.astype(jnp.bfloat16)


def contract(row_blocks, occupied_row, virtual_rows):
    ri_count = row_blocks.shape[2]
    blocks = row_blocks.reshape(3, 3, ri_count, BO, BO).astype(jnp.float32)
    occupied_blocks = occupied_row.reshape(3, BO, BO).astype(jnp.float32)
    virtual_blocks = virtual_rows.reshape(3, 3, BO, BO).astype(jnp.float32)
    occupied_terms = []
    virtual_terms = []
    for out_band in range(5):
        total_left = jnp.zeros((ri_count, BO, BO), jnp.float32)
        total_right = jnp.zeros((ri_count, BO, BO), jnp.float32)
        for left_band in range(3):
            right_band = out_band - left_band
            if 0 <= right_band < 3:
                total_left = total_left + jnp.einsum('lm,pmn->pln', occupied_blocks[left_band], blocks[left_band, right_band])
                total_right = total_right + jnp.einsum('pls,sn->pln', blocks[1, left_band], virtual_blocks[left_band, right_band])
        occupied_terms.append(total_left.reshape(ri_count, BO * BO))
        virtual_terms.append(total_right.reshape(ri_count, BO * BO))
    left_product = jnp.stack(occupied_terms, 1).reshape(ri_count, 5 * BO * BO).astype(jnp.bfloat16)
    right_product = jnp.stack(virtual_terms, 1).reshape(ri_count, 5 * BO * BO).astype(jnp.bfloat16)
    return left_product, right_product


def reference(tensor, occupied, virtual, atom_size, tensor_pattern, occupied_pattern, virtual_pattern):
    padded = jnp.pad(tensor, ((1, 1), (0, 0), (0, 0), (0, 0)))
    occupied_pad = jnp.pad(occupied, ((1, 1), (0, 0), (0, 0)))
    virtual_pad = jnp.pad(virtual, ((1, 1), (0, 0), (0, 0)))
    size_pad = jnp.pad(atom_size, 2)
    tensor_flags = jnp.pad(tensor_pattern, ((2, 2), (0, 0)))
    occupied_flags = jnp.pad(occupied_pattern, ((2, 2), (0, 0)))
    virtual_flags = jnp.pad(virtual_pattern, ((2, 2), (0, 0)))

    def advance(response, atom_index):
        row_blocks = lax.dynamic_slice_in_dim(padded, atom_index, 3, 0)
        tensor_mask, occupied_mask, virtual_mask = block_masks(size_pad, tensor_flags, occupied_flags, virtual_flags, atom_index)
        row_blocks = row_blocks * tensor_mask
        occupied_row = lax.dynamic_slice_in_dim(occupied_pad, atom_index + 1, 1, 0)[0] * occupied_mask[:, None]
        virtual_rows = lax.dynamic_slice_in_dim(virtual_pad, atom_index, 3, 0) * virtual_mask[:, :, None]
        left_product, right_product = contract(row_blocks, occupied_row, virtual_rows)
        return response + jnp.dot(left_product, right_product.T, preferred_element_type=jnp.float32), None

    response, unused = lax.scan(advance, jnp.zeros((PCH, PCH), jnp.float32), jnp.arange(NA, dtype=jnp.int32))
    return response
```

```python
import jax
import jax.numpy as jnp
from jax import lax
from jax.sharding import PartitionSpec as P

BO = 32


def with_halo(array, sides, width):
    for axis, dim in sides:
        devices, length = (lax.axis_size(axis), array.shape[dim])
        up = [(i, (i + 1) % devices) for i in range(devices - 1)]
        down = [(j, i) for i, j in up]
        last = lax.slice_in_dim(array, length - width, length, axis=dim)
        initial = lax.slice_in_dim(array, 0, width, axis=dim)
        before = lax.ppermute(last, axis, up)
        after = lax.ppermute(initial, axis, down)
        array = jnp.concatenate([before, array, after], axis=dim)
    return array


def block_masks(size_pad, tensor_flags, occupied_flags, virtual_flags, atom_index):
    nearby_sizes = lax.dynamic_slice(size_pad, (atom_index,), (5,))
    present = (nearby_sizes > 0).astype(jnp.int32)
    orbital = jnp.arange(BO, dtype=jnp.int32)
    zero_index = jnp.zeros((), jnp.int32)
    row_flags = lax.dynamic_slice(tensor_flags, (atom_index + 1, zero_index), (3, 3))
    row_ok = (orbital[None, :] < nearby_sizes[1:4, None]).astype(jnp.int32)
    partner = jnp.stack([nearby_sizes[r : r + 3] for r in range(3)])
    column_ok = (orbital[None, None, :] < partner[:, :, None]).astype(jnp.int32)
    entry_mask = row_flags[:, :, None, None] * row_ok[:, None, :, None] * column_ok[:, :, None, :]
    tensor_mask = entry_mask.reshape(3, 3, 1, BO * BO).astype(jnp.bfloat16)
    occupied_mask = (
        lax.dynamic_slice(occupied_flags, (atom_index + 2, zero_index), (1, 3))[0] * present[1:4]
    )
    partner_present = jnp.stack([present[r : r + 3] for r in range(3)])
    virtual_mask = (
        lax.dynamic_slice(virtual_flags, (atom_index + 1, zero_index), (3, 3))
        * present[1:4, None]
        * partner_present
    )
    return (tensor_mask, occupied_mask.astype(jnp.bfloat16), virtual_mask.astype(jnp.bfloat16))


def contract(row_blocks, occupied_row, virtual_rows):
    ri_count = row_blocks.shape[2]
    blocks = row_blocks.reshape(3, 3, ri_count, BO, BO)
    occupied_blocks = occupied_row.reshape(3, BO, BO)
    virtual_blocks = virtual_rows.reshape(3, 3, BO, BO)
    occupied_terms = []
    virtual_terms = []
    for out_band in range(5):
        total_left = jnp.zeros((ri_count, BO, BO), jnp.float32)
        total_right = jnp.zeros((ri_count, BO, BO), jnp.float32)
        for left_band in range(3):
            right_band = out_band - left_band
            if 0 <= right_band < 3:
                total_left = total_left + jnp.einsum(
                    "lm,pmn->pln",
                    occupied_blocks[left_band],
                    blocks[left_band, right_band],
                    preferred_element_type=jnp.float32,
                )
                total_right = total_right + jnp.einsum(
                    "pls,sn->pln",
                    blocks[1, left_band],
                    virtual_blocks[left_band, right_band],
                    preferred_element_type=jnp.float32,
                )
        occupied_terms.append(total_left.reshape(ri_count, BO * BO))
        virtual_terms.append(total_right.reshape(ri_count, BO * BO))
    left_product = jnp.stack(occupied_terms, 1).reshape(ri_count, 5 * BO * BO).astype(jnp.bfloat16)
    right_product = jnp.stack(virtual_terms, 1).reshape(ri_count, 5 * BO * BO).astype(jnp.bfloat16)
    return (left_product, right_product)


def body(tensor, occupied, virtual, atom_size, tensor_pattern, occupied_pattern, virtual_pattern):
    narrow_count = lax.axis_size("narrow")
    atom_index = lax.axis_index("wide") * narrow_count + lax.axis_index("narrow")
    sectioned_rows = tensor[:, None]
    regrouped = lax.all_to_all(sectioned_rows, "narrow", split_axis=0, concat_axis=3, tiled=True)
    row_blocks = with_halo(regrouped[:, 0], ((("wide", "narrow"), 0),), 1)
    occupied_pad = jnp.pad(occupied, ((1, 1), (0, 0), (0, 0)))
    virtual_pad = jnp.pad(virtual, ((1, 1), (0, 0), (0, 0)))
    size_pad = jnp.pad(atom_size, 2)
    tensor_flags = jnp.pad(tensor_pattern, ((2, 2), (0, 0)))
    occupied_flags = jnp.pad(occupied_pattern, ((2, 2), (0, 0)))
    virtual_flags = jnp.pad(virtual_pattern, ((2, 2), (0, 0)))
    tensor_mask, occupied_mask, virtual_mask = block_masks(
        size_pad, tensor_flags, occupied_flags, virtual_flags, atom_index
    )
    row_blocks = row_blocks * tensor_mask
    occupied_row = (
        lax.dynamic_slice_in_dim(occupied_pad, atom_index + 1, 1, 0)[0] * occupied_mask[:, None]
    )
    virtual_rows = (
        lax.dynamic_slice_in_dim(virtual_pad, atom_index, 3, 0) * virtual_mask[:, :, None]
    )
    left_product, right_product = contract(row_blocks, occupied_row, virtual_rows)
    partial_response = lax.dot_general(
        left_product, right_product, (((1,), (1,)), ((), ())), preferred_element_type=jnp.float32
    )
    column_share = lax.psum_scatter(partial_response, "narrow", scatter_dimension=1, tiled=True)
    wide_count = lax.axis_size("wide")
    row_pieces = column_share.reshape(wide_count, column_share.shape[0] // wide_count, column_share.shape[1])
    gathered = lax.all_to_all(row_pieces, "wide", 0, 0, tiled=True)
    return gathered.sum(0)


def solution(mesh):
    placed = (P("wide", None, "narrow", None), P(), P(), P(), P(), P(), P())
    return jax.shard_map(
        body, mesh=mesh, in_specs=placed, out_specs=P("wide", "narrow"), check_vma=False
    )
```

```python
import jax
import jax.numpy as jnp
from jax import lax
from jax.sharding import PartitionSpec as P

BO = 32


def block_masks(size_pad, tensor_flags, occupied_flags, virtual_flags, atom_index):
    nearby_sizes = lax.dynamic_slice(size_pad, (atom_index,), (5,))
    present = (nearby_sizes > 0).astype(jnp.int32)
    orbital = jnp.arange(BO, dtype=jnp.int32)
    zero_index = jnp.zeros((), jnp.int32)
    row_flags = lax.dynamic_slice(tensor_flags, (atom_index + 1, zero_index), (3, 3))
    row_ok = (orbital[None, :] < nearby_sizes[1:4, None]).astype(jnp.int32)
    partner = jnp.stack([nearby_sizes[r : r + 3] for r in range(3)])
    column_ok = (orbital[None, None, :] < partner[:, :, None]).astype(jnp.int32)
    entry_mask = row_flags[:, :, None, None] * row_ok[:, None, :, None] * column_ok[:, :, None, :]
    tensor_mask = entry_mask.reshape(3, 3, 1, BO * BO).astype(jnp.bfloat16)
    occupied_mask = (
        lax.dynamic_slice(occupied_flags, (atom_index + 2, zero_index), (1, 3))[0] * present[1:4]
    )
    partner_present = jnp.stack([present[r : r + 3] for r in range(3)])
    virtual_mask = (
        lax.dynamic_slice(virtual_flags, (atom_index + 1, zero_index), (3, 3))
        * present[1:4, None]
        * partner_present
    )
    return (tensor_mask, occupied_mask.astype(jnp.bfloat16), virtual_mask.astype(jnp.bfloat16))


def left_kron(block, row_mask):
    identity = jnp.eye(BO, dtype=jnp.float32)
    full = (block.T[:, None, :, None] * identity[None, :, None, :]).reshape(BO * BO, BO * BO)
    return (full * row_mask[:, None]).astype(jnp.bfloat16)


def right_kron(block, row_mask):
    identity = jnp.eye(BO, dtype=jnp.float32)
    full = (identity[:, None, :, None] * block[None, :, None, :]).reshape(BO * BO, BO * BO)
    return (full * row_mask[:, None]).astype(jnp.bfloat16)


def contract(rows, tensor_mask, occupied_row, virtual_rows):
    occupied_blocks = occupied_row.reshape(3, BO, BO).astype(jnp.float32)
    virtual_blocks = virtual_rows.reshape(3, 3, BO, BO).astype(jnp.float32)
    row_masks = tensor_mask.reshape(3, 3, BO * BO).astype(jnp.float32)
    occupied_terms = []
    virtual_terms = []
    for out_band in range(5):
        total_left = None
        total_right = None
        for left_band in range(3):
            right_band = out_band - left_band
            if 0 <= right_band < 3:
                left = jnp.dot(
                    rows[left_band][right_band],
                    left_kron(occupied_blocks[left_band], row_masks[left_band, right_band]),
                    preferred_element_type=jnp.float32,
                )
                right = jnp.dot(
                    rows[1][left_band],
                    right_kron(virtual_blocks[left_band, right_band], row_masks[1, left_band]),
                    preferred_element_type=jnp.float32,
                )
                total_left = left if total_left is None else total_left + left
                total_right = right if total_right is None else total_right + right
        occupied_terms.append(total_left.astype(jnp.bfloat16))
        virtual_terms.append(total_right.astype(jnp.bfloat16))
    left_product = jnp.concatenate(occupied_terms, 1)
    right_product = jnp.concatenate(virtual_terms, 1)
    return (left_product, right_product)


def neighbours(array, axis):
    devices = lax.axis_size(axis)
    up = [(i, (i + 1) % devices) for i in range(devices - 1)]
    down = [(j, i) for i, j in up]
    before = lax.ppermute(array, axis, up)
    after = lax.ppermute(array, axis, down)
    return before, after


def body(tensor, occupied, virtual, atom_size, tensor_pattern, occupied_pattern, virtual_pattern):
    narrow_count = lax.axis_size("narrow")
    atom_index = lax.axis_index("wide") * narrow_count + lax.axis_index("narrow")
    sectioned_rows = tensor[:, None]
    regrouped = lax.all_to_all(sectioned_rows, "narrow", split_axis=0, concat_axis=3, tiled=True)
    own = regrouped[0, 0]
    before, after = neighbours(own, ("wide", "narrow"))
    occupied_pad = jnp.pad(occupied, ((1, 1), (0, 0), (0, 0)))
    virtual_pad = jnp.pad(virtual, ((1, 1), (0, 0), (0, 0)))
    size_pad = jnp.pad(atom_size, 2)
    tensor_flags = jnp.pad(tensor_pattern, ((2, 2), (0, 0)))
    occupied_flags = jnp.pad(occupied_pattern, ((2, 2), (0, 0)))
    virtual_flags = jnp.pad(virtual_pattern, ((2, 2), (0, 0)))
    tensor_mask, occupied_mask, virtual_mask = block_masks(
        size_pad, tensor_flags, occupied_flags, virtual_flags, atom_index
    )
    occupied_row = (
        lax.dynamic_slice_in_dim(occupied_pad, atom_index + 1, 1, 0)[0] * occupied_mask[:, None]
    )
    virtual_rows = (
        lax.dynamic_slice_in_dim(virtual_pad, atom_index, 3, 0) * virtual_mask[:, :, None]
    )
    left_product, right_product = contract(
        (before, own, after), tensor_mask, occupied_row, virtual_rows
    )
    partial_response = lax.dot_general(
        left_product, right_product, (((1,), (1,)), ((), ())), preferred_element_type=jnp.float32
    )
    column_share = lax.psum_scatter(partial_response, "narrow", scatter_dimension=1, tiled=True)
    wide_count = lax.axis_size("wide")
    row_pieces = column_share.reshape(wide_count, column_share.shape[0] // wide_count, column_share.shape[1])
    gathered = lax.all_to_all(row_pieces, "wide", 0, 0, tiled=True)
    return gathered.sum(0)


def solution(mesh):
    placed = (P("wide", None, "narrow", None), P(), P(), P(), P(), P(), P())
    return jax.shard_map(
        body, mesh=mesh, in_specs=placed, out_specs=P("wide", "narrow"), check_vma=False
    )
```

```python
import jax
import jax.numpy as jnp
from jax import lax
from jax.sharding import PartitionSpec as P

BO = 32


def block_masks(size_pad, tensor_flags, occupied_flags, virtual_flags, atom_index):
    nearby_sizes = lax.dynamic_slice(size_pad, (atom_index,), (5,))
    present = (nearby_sizes > 0).astype(jnp.int32)
    orbital = jnp.arange(BO, dtype=jnp.int32)
    zero_index = jnp.zeros((), jnp.int32)
    row_flags = lax.dynamic_slice(tensor_flags, (atom_index + 1, zero_index), (3, 3))
    row_ok = (orbital[None, :] < nearby_sizes[1:4, None]).astype(jnp.int32)
    partner = jnp.stack([nearby_sizes[r : r + 3] for r in range(3)])
    column_ok = (orbital[None, None, :] < partner[:, :, None]).astype(jnp.int32)
    entry_mask = row_flags[:, :, None, None] * row_ok[:, None, :, None] * column_ok[:, :, None, :]
    tensor_mask = entry_mask.reshape(3, 3, 1, BO * BO).astype(jnp.bfloat16)
    occupied_mask = (
        lax.dynamic_slice(occupied_flags, (atom_index + 2, zero_index), (1, 3))[0] * present[1:4]
    )
    partner_present = jnp.stack([present[r : r + 3] for r in range(3)])
    virtual_mask = (
        lax.dynamic_slice(virtual_flags, (atom_index + 1, zero_index), (3, 3))
        * present[1:4, None]
        * partner_present
    )
    return (tensor_mask, occupied_mask.astype(jnp.bfloat16), virtual_mask.astype(jnp.bfloat16))


def left_kron(block, row_mask):
    size = BO * BO
    spread = jnp.repeat(block.T, BO, axis=1)
    full = jnp.broadcast_to(spread[:, None, :], (BO, BO, size)).reshape(size, size)
    rows = lax.broadcasted_iota(jnp.int32, (size, size), 0)
    columns = lax.broadcasted_iota(jnp.int32, (size, size), 1)
    keep = (rows % BO) == (columns % BO)
    return (jnp.where(keep, full, 0.0) * row_mask[:, None]).astype(jnp.bfloat16)


def right_kron(block, row_mask):
    size = BO * BO
    spread = jnp.tile(block, (1, BO))
    full = jnp.broadcast_to(spread[None, :, :], (BO, BO, size)).reshape(size, size)
    rows = lax.broadcasted_iota(jnp.int32, (size, size), 0)
    columns = lax.broadcasted_iota(jnp.int32, (size, size), 1)
    keep = (rows // BO) == (columns // BO)
    return (jnp.where(keep, full, 0.0) * row_mask[:, None]).astype(jnp.bfloat16)


def contract(rows, tensor_mask, occupied_row, virtual_rows):
    occupied_blocks = occupied_row.reshape(3, BO, BO).astype(jnp.float32)
    virtual_blocks = virtual_rows.reshape(3, 3, BO, BO).astype(jnp.float32)
    row_masks = tensor_mask.reshape(3, 3, BO * BO).astype(jnp.float32)
    occupied_terms = []
    virtual_terms = []
    for out_band in range(5):
        total_left = None
        total_right = None
        for left_band in range(3):
            right_band = out_band - left_band
            if 0 <= right_band < 3:
                left = jnp.dot(
                    rows[left_band][right_band],
                    left_kron(occupied_blocks[left_band], row_masks[left_band, right_band]),
                    preferred_element_type=jnp.float32,
                )
                right = jnp.dot(
                    rows[1][left_band],
                    right_kron(virtual_blocks[left_band, right_band], row_masks[1, left_band]),
                    preferred_element_type=jnp.float32,
                )
                total_left = left if total_left is None else total_left + left
                total_right = right if total_right is None else total_right + right
        occupied_terms.append(total_left.astype(jnp.bfloat16))
        virtual_terms.append(total_right.astype(jnp.bfloat16))
    left_product = jnp.concatenate(occupied_terms, 1)
    right_product = jnp.concatenate(virtual_terms, 1)
    return (left_product, right_product)


def neighbours(array, axis):
    devices = lax.axis_size(axis)
    up = [(i, (i + 1) % devices) for i in range(devices - 1)]
    down = [(j, i) for i, j in up]
    before = lax.ppermute(array, axis, up)
    after = lax.ppermute(array, axis, down)
    return before, after


def body(tensor, occupied, virtual, atom_size, tensor_pattern, occupied_pattern, virtual_pattern):
    narrow_count = lax.axis_size("narrow")
    atom_index = lax.axis_index("wide") * narrow_count + lax.axis_index("narrow")
    sectioned_rows = tensor[:, None]
    regrouped = lax.all_to_all(sectioned_rows, "narrow", split_axis=0, concat_axis=3, tiled=True)
    own = regrouped[0, 0]
    before, after = neighbours(own, ("wide", "narrow"))
    occupied_pad = jnp.pad(occupied, ((1, 1), (0, 0), (0, 0)))
    virtual_pad = jnp.pad(virtual, ((1, 1), (0, 0), (0, 0)))
    size_pad = jnp.pad(atom_size, 2)
    tensor_flags = jnp.pad(tensor_pattern, ((2, 2), (0, 0)))
    occupied_flags = jnp.pad(occupied_pattern, ((2, 2), (0, 0)))
    virtual_flags = jnp.pad(virtual_pattern, ((2, 2), (0, 0)))
    tensor_mask, occupied_mask, virtual_mask = block_masks(
        size_pad, tensor_flags, occupied_flags, virtual_flags, atom_index
    )
    occupied_row = (
        lax.dynamic_slice_in_dim(occupied_pad, atom_index + 1, 1, 0)[0] * occupied_mask[:, None]
    )
    virtual_rows = (
        lax.dynamic_slice_in_dim(virtual_pad, atom_index, 3, 0) * virtual_mask[:, :, None]
    )
    left_product, right_product = contract(
        (before, own, after), tensor_mask, occupied_row, virtual_rows
    )
    partial_response = lax.dot_general(
        left_product, right_product, (((1,), (1,)), ((), ())), preferred_element_type=jnp.float32
    )
    column_share = lax.psum_scatter(partial_response, "narrow", scatter_dimension=1, tiled=True)
    wide_count = lax.axis_size("wide")
    row_pieces = column_share.reshape(wide_count, column_share.shape[0] // wide_count, column_share.shape[1])
    gathered = lax.all_to_all(row_pieces, "wide", 0, 0, tiled=True)
    return gathered.sum(0)


def solution(mesh):
    placed = (P("wide", None, "narrow", None), P(), P(), P(), P(), P(), P())
    return jax.shard_map(
        body, mesh=mesh, in_specs=placed, out_specs=P("wide", "narrow"), check_vma=False
    )
```

```python
import jax
import jax.numpy as jnp
from jax import lax
from jax.sharding import PartitionSpec as P

BO = 32
CHUNK = 256


def block_masks(size_pad, tensor_flags, occupied_flags, virtual_flags, atom_index):
    nearby_sizes = lax.dynamic_slice(size_pad, (atom_index,), (5,))
    present = (nearby_sizes > 0).astype(jnp.int32)
    orbital = jnp.arange(BO, dtype=jnp.int32)
    zero_index = jnp.zeros((), jnp.int32)
    row_flags = lax.dynamic_slice(tensor_flags, (atom_index + 1, zero_index), (3, 3))
    row_ok = (orbital[None, :] < nearby_sizes[1:4, None]).astype(jnp.int32)
    partner = jnp.stack([nearby_sizes[r : r + 3] for r in range(3)])
    column_ok = (orbital[None, None, :] < partner[:, :, None]).astype(jnp.int32)
    entry_mask = row_flags[:, :, None, None] * row_ok[:, None, :, None] * column_ok[:, :, None, :]
    tensor_mask = entry_mask.reshape(3, 3, 1, BO * BO).astype(jnp.bfloat16)
    occupied_mask = (
        lax.dynamic_slice(occupied_flags, (atom_index + 2, zero_index), (1, 3))[0] * present[1:4]
    )
    partner_present = jnp.stack([present[r : r + 3] for r in range(3)])
    virtual_mask = (
        lax.dynamic_slice(virtual_flags, (atom_index + 1, zero_index), (3, 3))
        * present[1:4, None]
        * partner_present
    )
    return (tensor_mask, occupied_mask.astype(jnp.bfloat16), virtual_mask.astype(jnp.bfloat16))


def left_kron(block, row_mask):
    size = BO * BO
    spread = jnp.repeat(block.T, BO, axis=1)
    full = jnp.broadcast_to(spread[:, None, :], (BO, BO, size)).reshape(size, size)
    rows = lax.broadcasted_iota(jnp.int32, (size, size), 0)
    columns = lax.broadcasted_iota(jnp.int32, (size, size), 1)
    keep = (rows % BO) == (columns % BO)
    return (jnp.where(keep, full, 0.0) * row_mask[:, None]).astype(jnp.bfloat16)


def right_kron(block, row_mask):
    size = BO * BO
    spread = jnp.tile(block, (1, BO))
    full = jnp.broadcast_to(spread[None, :, :], (BO, BO, size)).reshape(size, size)
    rows = lax.broadcasted_iota(jnp.int32, (size, size), 0)
    columns = lax.broadcasted_iota(jnp.int32, (size, size), 1)
    keep = (rows // BO) == (columns // BO)
    return (jnp.where(keep, full, 0.0) * row_mask[:, None]).astype(jnp.bfloat16)


def right_kron_chunks(block, row_mask, chunk):
    groups = chunk // BO
    spread = jnp.tile(block, (1, groups))
    full = jnp.broadcast_to(spread[None, :, :], (groups, BO, chunk)).reshape(chunk, chunk)
    rows = lax.broadcasted_iota(jnp.int32, (chunk, chunk), 0)
    columns = lax.broadcasted_iota(jnp.int32, (chunk, chunk), 1)
    keep = (rows // BO) == (columns // BO)
    sized = jnp.where(keep, full, 0.0)
    masks = row_mask.reshape(-1, chunk)
    return (sized[None] * masks[:, :, None]).astype(jnp.bfloat16)


def contract(rows, tensor_mask, occupied_row, virtual_rows):
    occupied_blocks = occupied_row.reshape(3, BO, BO).astype(jnp.float32)
    virtual_blocks = virtual_rows.reshape(3, 3, BO, BO).astype(jnp.float32)
    row_masks = tensor_mask.reshape(3, 3, BO * BO).astype(jnp.float32)
    occupied_terms = []
    virtual_terms = []
    for out_band in range(5):
        total_left = None
        total_right = None
        for left_band in range(3):
            right_band = out_band - left_band
            if 0 <= right_band < 3:
                left = jnp.dot(
                    rows[left_band][right_band],
                    left_kron(occupied_blocks[left_band], row_masks[left_band, right_band]),
                    preferred_element_type=jnp.float32,
                )
                source = rows[1][left_band]
                right = jnp.einsum(
                    "pcj,cjk->pck",
                    source.reshape(source.shape[0], -1, CHUNK),
                    right_kron_chunks(virtual_blocks[left_band, right_band], row_masks[1, left_band], CHUNK),
                    preferred_element_type=jnp.float32,
                ).reshape(source.shape)
                total_left = left if total_left is None else total_left + left
                total_right = right if total_right is None else total_right + right
        occupied_terms.append(total_left.astype(jnp.bfloat16))
        virtual_terms.append(total_right.astype(jnp.bfloat16))
    left_product = jnp.concatenate(occupied_terms, 1)
    right_product = jnp.concatenate(virtual_terms, 1)
    return (left_product, right_product)


def neighbours(array, axis):
    devices = lax.axis_size(axis)
    up = [(i, (i + 1) % devices) for i in range(devices - 1)]
    down = [(j, i) for i, j in up]
    before = lax.ppermute(array, axis, up)
    after = lax.ppermute(array, axis, down)
    return before, after


def body(tensor, occupied, virtual, atom_size, tensor_pattern, occupied_pattern, virtual_pattern):
    narrow_count = lax.axis_size("narrow")
    atom_index = lax.axis_index("wide") * narrow_count + lax.axis_index("narrow")
    sectioned_rows = tensor[:, None]
    regrouped = lax.all_to_all(sectioned_rows, "narrow", split_axis=0, concat_axis=3, tiled=True)
    own = regrouped[0, 0]
    before, after = neighbours(own, ("wide", "narrow"))
    occupied_pad = jnp.pad(occupied, ((1, 1), (0, 0), (0, 0)))
    virtual_pad = jnp.pad(virtual, ((1, 1), (0, 0), (0, 0)))
    size_pad = jnp.pad(atom_size, 2)
    tensor_flags = jnp.pad(tensor_pattern, ((2, 2), (0, 0)))
    occupied_flags = jnp.pad(occupied_pattern, ((2, 2), (0, 0)))
    virtual_flags = jnp.pad(virtual_pattern, ((2, 2), (0, 0)))
    tensor_mask, occupied_mask, virtual_mask = block_masks(
        size_pad, tensor_flags, occupied_flags, virtual_flags, atom_index
    )
    occupied_row = (
        lax.dynamic_slice_in_dim(occupied_pad, atom_index + 1, 1, 0)[0] * occupied_mask[:, None]
    )
    virtual_rows = (
        lax.dynamic_slice_in_dim(virtual_pad, atom_index, 3, 0) * virtual_mask[:, :, None]
    )
    left_product, right_product = contract(
        (before, own, after), tensor_mask, occupied_row, virtual_rows
    )
    partial_response = lax.dot_general(
        left_product, right_product, (((1,), (1,)), ((), ())), preferred_element_type=jnp.float32
    )
    column_share = lax.psum_scatter(partial_response, "narrow", scatter_dimension=1, tiled=True)
    wide_count = lax.axis_size("wide")
    row_pieces = column_share.reshape(wide_count, column_share.shape[0] // wide_count, column_share.shape[1])
    gathered = lax.all_to_all(row_pieces, "wide", 0, 0, tiled=True)
    return gathered.sum(0)


def solution(mesh):
    placed = (P("wide", None, "narrow", None), P(), P(), P(), P(), P(), P())
    return jax.shard_map(
        body, mesh=mesh, in_specs=placed, out_specs=P("wide", "narrow"), check_vma=False
    )
```

```python
import jax
import jax.numpy as jnp
from jax import lax
from jax.sharding import PartitionSpec as P

BO = 32
CHUNK = 256


def block_masks(size_pad, tensor_flags, occupied_flags, virtual_flags, atom_index):
    nearby_sizes = lax.dynamic_slice(size_pad, (atom_index,), (5,))
    present = (nearby_sizes > 0).astype(jnp.int32)
    orbital = jnp.arange(BO, dtype=jnp.int32)
    zero_index = jnp.zeros((), jnp.int32)
    row_flags = lax.dynamic_slice(tensor_flags, (atom_index + 1, zero_index), (3, 3))
    row_ok = (orbital[None, :] < nearby_sizes[1:4, None]).astype(jnp.int32)
    partner = jnp.stack([nearby_sizes[r : r + 3] for r in range(3)])
    column_ok = (orbital[None, None, :] < partner[:, :, None]).astype(jnp.int32)
    entry_mask = row_flags[:, :, None, None] * row_ok[:, None, :, None] * column_ok[:, :, None, :]
    tensor_mask = entry_mask.reshape(3, 3, 1, BO * BO).astype(jnp.bfloat16)
    occupied_mask = (
        lax.dynamic_slice(occupied_flags, (atom_index + 2, zero_index), (1, 3))[0] * present[1:4]
    )
    partner_present = jnp.stack([present[r : r + 3] for r in range(3)])
    virtual_mask = (
        lax.dynamic_slice(virtual_flags, (atom_index + 1, zero_index), (3, 3))
        * present[1:4, None]
        * partner_present
    )
    return (tensor_mask, occupied_mask.astype(jnp.bfloat16), virtual_mask.astype(jnp.bfloat16))


def left_kron(block, row_mask):
    size = BO * BO
    spread = jnp.repeat(block.T, BO, axis=1)
    full = jnp.broadcast_to(spread[:, None, :], (BO, BO, size)).reshape(size, size)
    rows = lax.broadcasted_iota(jnp.int32, (size, size), 0)
    columns = lax.broadcasted_iota(jnp.int32, (size, size), 1)
    keep = (rows % BO) == (columns % BO)
    return (jnp.where(keep, full, 0.0) * row_mask[:, None]).astype(jnp.bfloat16)


def right_kron(block, row_mask):
    size = BO * BO
    spread = jnp.tile(block, (1, BO))
    full = jnp.broadcast_to(spread[None, :, :], (BO, BO, size)).reshape(size, size)
    rows = lax.broadcasted_iota(jnp.int32, (size, size), 0)
    columns = lax.broadcasted_iota(jnp.int32, (size, size), 1)
    keep = (rows // BO) == (columns // BO)
    return (jnp.where(keep, full, 0.0) * row_mask[:, None]).astype(jnp.bfloat16)


def right_kron_chunks(block, row_mask, chunk):
    groups = chunk // BO
    spread = jnp.tile(block, (1, groups))
    full = jnp.broadcast_to(spread[None, :, :], (groups, BO, chunk)).reshape(chunk, chunk)
    rows = lax.broadcasted_iota(jnp.int32, (chunk, chunk), 0)
    columns = lax.broadcasted_iota(jnp.int32, (chunk, chunk), 1)
    keep = (rows // BO) == (columns // BO)
    sized = jnp.where(keep, full, 0.0)
    masks = row_mask.reshape(-1, chunk)
    return (sized[None] * masks[:, :, None]).astype(jnp.bfloat16)


def contract(rows, tensor_mask, occupied_row, virtual_rows):
    occupied_blocks = occupied_row.reshape(3, BO, BO).astype(jnp.float32)
    virtual_blocks = virtual_rows.reshape(3, 3, BO, BO).astype(jnp.float32)
    row_masks = tensor_mask.reshape(3, 3, BO * BO).astype(jnp.float32)
    occupied_terms = []
    virtual_terms = []
    for out_band in range(5):
        total_left = None
        total_right = None
        for left_band in range(3):
            right_band = out_band - left_band
            if 0 <= right_band < 3:
                left = jnp.dot(
                    rows[left_band][right_band],
                    left_kron(occupied_blocks[left_band], row_masks[left_band, right_band]),
                    preferred_element_type=jnp.float32,
                )
                source = rows[1][left_band]
                right = jnp.einsum(
                    "pcj,cjk->pck",
                    source.reshape(source.shape[0], -1, CHUNK),
                    right_kron_chunks(virtual_blocks[left_band, right_band], row_masks[1, left_band], CHUNK),
                    preferred_element_type=jnp.float32,
                ).reshape(source.shape)
                total_left = left if total_left is None else total_left + left
                total_right = right if total_right is None else total_right + right
        occupied_terms.append(total_left.astype(jnp.bfloat16))
        virtual_terms.append(total_right.astype(jnp.bfloat16))
    left_product = jnp.concatenate(occupied_terms, 1)
    right_product = jnp.concatenate(virtual_terms, 1)
    return (left_product, right_product)


def neighbours(array, axis):
    devices = lax.axis_size(axis)
    up = [(i, (i + 1) % devices) for i in range(devices - 1)]
    down = [(j, i) for i, j in up]
    before = lax.ppermute(array, axis, up)
    after = lax.ppermute(array, axis, down)
    return before, after


def halving_scatter(partial, axis):
    devices = lax.axis_size(axis)
    me = lax.axis_index(axis)
    rows = partial.shape[0]
    held = partial.reshape(rows, devices, partial.shape[1] // devices)
    bit = 1
    while bit < devices:
        groups = held.shape[1] // 2
        pairs = held.reshape(rows, groups, 2, held.shape[2])
        mine = (me // bit) % 2
        keep = lax.dynamic_index_in_dim(pairs, mine, 2, keepdims=False)
        give = lax.dynamic_index_in_dim(pairs, 1 - mine, 2, keepdims=False)
        partner = [(i, i ^ bit) for i in range(devices)]
        held = keep + lax.ppermute(give, axis, partner)
        bit *= 2
    return held.reshape(rows, held.shape[2])


def body(tensor, occupied, virtual, atom_size, tensor_pattern, occupied_pattern, virtual_pattern):
    narrow_count = lax.axis_size("narrow")
    atom_index = lax.axis_index("wide") * narrow_count + lax.axis_index("narrow")
    sectioned_rows = tensor[:, None]
    regrouped = lax.all_to_all(sectioned_rows, "narrow", split_axis=0, concat_axis=3, tiled=True)
    own = regrouped[0, 0]
    before, after = neighbours(own, ("wide", "narrow"))
    occupied_pad = jnp.pad(occupied, ((1, 1), (0, 0), (0, 0)))
    virtual_pad = jnp.pad(virtual, ((1, 1), (0, 0), (0, 0)))
    size_pad = jnp.pad(atom_size, 2)
    tensor_flags = jnp.pad(tensor_pattern, ((2, 2), (0, 0)))
    occupied_flags = jnp.pad(occupied_pattern, ((2, 2), (0, 0)))
    virtual_flags = jnp.pad(virtual_pattern, ((2, 2), (0, 0)))
    tensor_mask, occupied_mask, virtual_mask = block_masks(
        size_pad, tensor_flags, occupied_flags, virtual_flags, atom_index
    )
    occupied_row = (
        lax.dynamic_slice_in_dim(occupied_pad, atom_index + 1, 1, 0)[0] * occupied_mask[:, None]
    )
    virtual_rows = (
        lax.dynamic_slice_in_dim(virtual_pad, atom_index, 3, 0) * virtual_mask[:, :, None]
    )
    left_product, right_product = contract(
        (before, own, after), tensor_mask, occupied_row, virtual_rows
    )
    partial_response = lax.dot_general(
        left_product, right_product, (((1,), (1,)), ((), ())), preferred_element_type=jnp.float32
    )
    column_share = halving_scatter(partial_response, "narrow")
    wide_count = lax.axis_size("wide")
    row_pieces = column_share.reshape(wide_count, column_share.shape[0] // wide_count, column_share.shape[1])
    gathered = lax.all_to_all(row_pieces, "wide", 0, 0, tiled=True)
    return gathered.sum(0)


def solution(mesh):
    placed = (P("wide", None, "narrow", None), P(), P(), P(), P(), P(), P())
    return jax.shard_map(
        body, mesh=mesh, in_specs=placed, out_specs=P("wide", "narrow"), check_vma=False
    )
```

```python
import jax
import jax.numpy as jnp
from jax import lax
from jax.sharding import PartitionSpec as P

BO = 32
CHUNK = 256


def block_masks(size_pad, tensor_flags, occupied_flags, virtual_flags, atom_index):
    nearby_sizes = lax.dynamic_slice(size_pad, (atom_index,), (5,))
    present = (nearby_sizes > 0).astype(jnp.int32)
    orbital = jnp.arange(BO, dtype=jnp.int32)
    zero_index = jnp.zeros((), jnp.int32)
    row_flags = lax.dynamic_slice(tensor_flags, (atom_index + 1, zero_index), (3, 3))
    row_ok = (orbital[None, :] < nearby_sizes[1:4, None]).astype(jnp.int32)
    partner = jnp.stack([nearby_sizes[r : r + 3] for r in range(3)])
    column_ok = (orbital[None, None, :] < partner[:, :, None]).astype(jnp.int32)
    entry_mask = row_flags[:, :, None, None] * row_ok[:, None, :, None] * column_ok[:, :, None, :]
    tensor_mask = entry_mask.reshape(3, 3, 1, BO * BO).astype(jnp.bfloat16)
    occupied_mask = (
        lax.dynamic_slice(occupied_flags, (atom_index + 2, zero_index), (1, 3))[0] * present[1:4]
    )
    partner_present = jnp.stack([present[r : r + 3] for r in range(3)])
    virtual_mask = (
        lax.dynamic_slice(virtual_flags, (atom_index + 1, zero_index), (3, 3))
        * present[1:4, None]
        * partner_present
    )
    return (tensor_mask, occupied_mask.astype(jnp.bfloat16), virtual_mask.astype(jnp.bfloat16))


def left_kron(block, row_mask):
    size = BO * BO
    spread = jnp.repeat(block.T, BO, axis=1)
    full = jnp.broadcast_to(spread[:, None, :], (BO, BO, size)).reshape(size, size)
    rows = lax.broadcasted_iota(jnp.int32, (size, size), 0)
    columns = lax.broadcasted_iota(jnp.int32, (size, size), 1)
    keep = (rows % BO) == (columns % BO)
    return (jnp.where(keep, full, 0.0) * row_mask[:, None]).astype(jnp.bfloat16)


def right_kron(block, row_mask):
    size = BO * BO
    spread = jnp.tile(block, (1, BO))
    full = jnp.broadcast_to(spread[None, :, :], (BO, BO, size)).reshape(size, size)
    rows = lax.broadcasted_iota(jnp.int32, (size, size), 0)
    columns = lax.broadcasted_iota(jnp.int32, (size, size), 1)
    keep = (rows // BO) == (columns // BO)
    return (jnp.where(keep, full, 0.0) * row_mask[:, None]).astype(jnp.bfloat16)


def right_kron_chunks(block, row_mask, chunk):
    groups = chunk // BO
    spread = jnp.tile(block, (1, groups))
    full = jnp.broadcast_to(spread[None, :, :], (groups, BO, chunk)).reshape(chunk, chunk)
    rows = lax.broadcasted_iota(jnp.int32, (chunk, chunk), 0)
    columns = lax.broadcasted_iota(jnp.int32, (chunk, chunk), 1)
    keep = (rows // BO) == (columns // BO)
    sized = jnp.where(keep, full, 0.0)
    masks = row_mask.reshape(-1, chunk)
    return (sized[None] * masks[:, :, None]).astype(jnp.bfloat16)


def contract(rows, tensor_mask, occupied_row, virtual_rows):
    occupied_blocks = occupied_row.reshape(3, BO, BO).astype(jnp.float32)
    virtual_blocks = virtual_rows.reshape(3, 3, BO, BO).astype(jnp.float32)
    row_masks = tensor_mask.reshape(3, 3, BO * BO).astype(jnp.float32)
    occupied_terms = []
    virtual_terms = []
    for out_band in range(5):
        total_left = None
        total_right = None
        for left_band in range(3):
            right_band = out_band - left_band
            if 0 <= right_band < 3:
                left = jnp.dot(
                    rows[left_band][right_band],
                    left_kron(occupied_blocks[left_band], row_masks[left_band, right_band]),
                    preferred_element_type=jnp.float32,
                )
                source = rows[1][left_band]
                pieces = right_kron_chunks(virtual_blocks[left_band, right_band], row_masks[1, left_band], CHUNK)
                right = jnp.concatenate(
                    [
                        jnp.dot(
                            source[:, piece * CHUNK : (piece + 1) * CHUNK],
                            pieces[piece],
                            preferred_element_type=jnp.float32,
                        )
                        for piece in range(pieces.shape[0])
                    ],
                    1,
                )
                total_left = left if total_left is None else total_left + left
                total_right = right if total_right is None else total_right + right
        occupied_terms.append(total_left.astype(jnp.bfloat16))
        virtual_terms.append(total_right.astype(jnp.bfloat16))
    left_product = jnp.concatenate(occupied_terms, 1)
    right_product = jnp.concatenate(virtual_terms, 1)
    return (left_product, right_product)


def neighbours(array, axis):
    devices = lax.axis_size(axis)
    up = [(i, (i + 1) % devices) for i in range(devices - 1)]
    down = [(j, i) for i, j in up]
    before = lax.ppermute(array, axis, up)
    after = lax.ppermute(array, axis, down)
    return before, after


def body(tensor, occupied, virtual, atom_size, tensor_pattern, occupied_pattern, virtual_pattern):
    narrow_count = lax.axis_size("narrow")
    atom_index = lax.axis_index("wide") * narrow_count + lax.axis_index("narrow")
    sectioned_rows = tensor[:, None]
    regrouped = lax.all_to_all(sectioned_rows, "narrow", split_axis=0, concat_axis=3, tiled=True)
    own = regrouped[0, 0]
    before, after = neighbours(own, ("wide", "narrow"))
    occupied_pad = jnp.pad(occupied, ((1, 1), (0, 0), (0, 0)))
    virtual_pad = jnp.pad(virtual, ((1, 1), (0, 0), (0, 0)))
    size_pad = jnp.pad(atom_size, 2)
    tensor_flags = jnp.pad(tensor_pattern, ((2, 2), (0, 0)))
    occupied_flags = jnp.pad(occupied_pattern, ((2, 2), (0, 0)))
    virtual_flags = jnp.pad(virtual_pattern, ((2, 2), (0, 0)))
    tensor_mask, occupied_mask, virtual_mask = block_masks(
        size_pad, tensor_flags, occupied_flags, virtual_flags, atom_index
    )
    occupied_row = (
        lax.dynamic_slice_in_dim(occupied_pad, atom_index + 1, 1, 0)[0] * occupied_mask[:, None]
    )
    virtual_rows = (
        lax.dynamic_slice_in_dim(virtual_pad, atom_index, 3, 0) * virtual_mask[:, :, None]
    )
    left_product, right_product = contract(
        (before, own, after), tensor_mask, occupied_row, virtual_rows
    )
    partial_response = lax.dot_general(
        left_product, right_product, (((1,), (1,)), ((), ())), preferred_element_type=jnp.float32
    )
    column_share = lax.psum_scatter(partial_response, "narrow", scatter_dimension=1, tiled=True)
    wide_count = lax.axis_size("wide")
    row_pieces = column_share.reshape(wide_count, column_share.shape[0] // wide_count, column_share.shape[1])
    gathered = lax.all_to_all(row_pieces, "wide", 0, 0, tiled=True)
    return gathered.sum(0)


def solution(mesh):
    placed = (P("wide", None, "narrow", None), P(), P(), P(), P(), P(), P())
    return jax.shard_map(
        body, mesh=mesh, in_specs=placed, out_specs=P("wide", "narrow"), check_vma=False
    )
```

```python
import jax
import jax.numpy as jnp
from jax import lax
from jax.sharding import PartitionSpec as P

BO = 32
CHUNK = 256


def block_masks(size_pad, tensor_flags, occupied_flags, virtual_flags, atom_index):
    nearby_sizes = lax.dynamic_slice(size_pad, (atom_index,), (5,))
    present = (nearby_sizes > 0).astype(jnp.int32)
    orbital = jnp.arange(BO, dtype=jnp.int32)
    zero_index = jnp.zeros((), jnp.int32)
    row_flags = lax.dynamic_slice(tensor_flags, (atom_index + 1, zero_index), (3, 3))
    row_ok = (orbital[None, :] < nearby_sizes[1:4, None]).astype(jnp.int32)
    partner = jnp.stack([nearby_sizes[r : r + 3] for r in range(3)])
    column_ok = (orbital[None, None, :] < partner[:, :, None]).astype(jnp.int32)
    entry_mask = row_flags[:, :, None, None] * row_ok[:, None, :, None] * column_ok[:, :, None, :]
    tensor_mask = entry_mask.reshape(3, 3, 1, BO * BO).astype(jnp.bfloat16)
    occupied_mask = (
        lax.dynamic_slice(occupied_flags, (atom_index + 2, zero_index), (1, 3))[0] * present[1:4]
    )
    partner_present = jnp.stack([present[r : r + 3] for r in range(3)])
    virtual_mask = (
        lax.dynamic_slice(virtual_flags, (atom_index + 1, zero_index), (3, 3))
        * present[1:4, None]
        * partner_present
    )
    return (tensor_mask, occupied_mask.astype(jnp.bfloat16), virtual_mask.astype(jnp.bfloat16))


def left_kron(block, row_mask):
    size = BO * BO
    spread = jnp.repeat(block.T, BO, axis=1)
    full = jnp.broadcast_to(spread[:, None, :], (BO, BO, size)).reshape(size, size)
    rows = lax.broadcasted_iota(jnp.int32, (size, size), 0)
    columns = lax.broadcasted_iota(jnp.int32, (size, size), 1)
    keep = (rows % BO) == (columns % BO)
    return (jnp.where(keep, full, 0.0) * row_mask[:, None]).astype(jnp.bfloat16)


def right_kron(block, row_mask):
    size = BO * BO
    spread = jnp.tile(block, (1, BO))
    full = jnp.broadcast_to(spread[None, :, :], (BO, BO, size)).reshape(size, size)
    rows = lax.broadcasted_iota(jnp.int32, (size, size), 0)
    columns = lax.broadcasted_iota(jnp.int32, (size, size), 1)
    keep = (rows // BO) == (columns // BO)
    return (jnp.where(keep, full, 0.0) * row_mask[:, None]).astype(jnp.bfloat16)


def right_kron_chunks(block, row_mask, chunk):
    groups = chunk // BO
    spread = jnp.tile(block, (1, groups))
    full = jnp.broadcast_to(spread[None, :, :], (groups, BO, chunk)).reshape(chunk, chunk)
    rows = lax.broadcasted_iota(jnp.int32, (chunk, chunk), 0)
    columns = lax.broadcasted_iota(jnp.int32, (chunk, chunk), 1)
    keep = (rows // BO) == (columns // BO)
    sized = jnp.where(keep, full, 0.0)
    masks = row_mask.reshape(-1, chunk)
    return (sized[None] * masks[:, :, None]).astype(jnp.bfloat16)


def contract(rows, tensor_mask, occupied_row, virtual_rows):
    occupied_blocks = occupied_row.reshape(3, BO, BO).astype(jnp.float32)
    virtual_blocks = virtual_rows.reshape(3, 3, BO, BO).astype(jnp.float32)
    row_masks = tensor_mask.reshape(3, 3, BO * BO).astype(jnp.float32)
    occupied_terms = []
    virtual_terms = []
    for out_band in range(5):
        total_left = None
        total_right = None
        for left_band in range(3):
            right_band = out_band - left_band
            if 0 <= right_band < 3:
                left = jnp.dot(
                    rows[left_band][right_band],
                    left_kron(occupied_blocks[left_band], row_masks[left_band, right_band]),
                    preferred_element_type=jnp.float32,
                )
                source = rows[1][left_band]
                pieces = right_kron_chunks(virtual_blocks[left_band, right_band], row_masks[1, left_band], CHUNK)
                right = jnp.concatenate(
                    [
                        jnp.dot(
                            source[:, piece * CHUNK : (piece + 1) * CHUNK],
                            pieces[piece],
                            preferred_element_type=jnp.float32,
                        )
                        for piece in range(pieces.shape[0])
                    ],
                    1,
                )
                total_left = left if total_left is None else total_left + left
                total_right = right if total_right is None else total_right + right
        occupied_terms.append(total_left.astype(jnp.bfloat16))
        virtual_terms.append(total_right.astype(jnp.bfloat16))
    return (occupied_terms, virtual_terms)


def neighbours(array, axis):
    devices = lax.axis_size(axis)
    up = [(i, (i + 1) % devices) for i in range(devices - 1)]
    down = [(j, i) for i, j in up]
    before = lax.ppermute(array, axis, up)
    after = lax.ppermute(array, axis, down)
    return before, after


def body(tensor, occupied, virtual, atom_size, tensor_pattern, occupied_pattern, virtual_pattern):
    narrow_count = lax.axis_size("narrow")
    atom_index = lax.axis_index("wide") * narrow_count + lax.axis_index("narrow")
    sectioned_rows = tensor[:, None]
    regrouped = lax.all_to_all(sectioned_rows, "narrow", split_axis=0, concat_axis=3, tiled=True)
    own = regrouped[0, 0]
    before, after = neighbours(own, ("wide", "narrow"))
    occupied_pad = jnp.pad(occupied, ((1, 1), (0, 0), (0, 0)))
    virtual_pad = jnp.pad(virtual, ((1, 1), (0, 0), (0, 0)))
    size_pad = jnp.pad(atom_size, 2)
    tensor_flags = jnp.pad(tensor_pattern, ((2, 2), (0, 0)))
    occupied_flags = jnp.pad(occupied_pattern, ((2, 2), (0, 0)))
    virtual_flags = jnp.pad(virtual_pattern, ((2, 2), (0, 0)))
    tensor_mask, occupied_mask, virtual_mask = block_masks(
        size_pad, tensor_flags, occupied_flags, virtual_flags, atom_index
    )
    occupied_row = (
        lax.dynamic_slice_in_dim(occupied_pad, atom_index + 1, 1, 0)[0] * occupied_mask[:, None]
    )
    virtual_rows = (
        lax.dynamic_slice_in_dim(virtual_pad, atom_index, 3, 0) * virtual_mask[:, :, None]
    )
    left_product, right_product = contract(
        (before, own, after), tensor_mask, occupied_row, virtual_rows
    )
    partial_response = None
    for left_band_product, right_band_product in zip(left_product, right_product):
        term = lax.dot_general(
            left_band_product, right_band_product, (((1,), (1,)), ((), ())), preferred_element_type=jnp.float32
        )
        partial_response = term if partial_response is None else partial_response + term
    column_share = lax.psum_scatter(partial_response, "narrow", scatter_dimension=1, tiled=True)
    wide_count = lax.axis_size("wide")
    row_pieces = column_share.reshape(wide_count, column_share.shape[0] // wide_count, column_share.shape[1])
    gathered = lax.all_to_all(row_pieces, "wide", 0, 0, tiled=True)
    return gathered.sum(0)


def solution(mesh):
    placed = (P("wide", None, "narrow", None), P(), P(), P(), P(), P(), P())
    return jax.shard_map(
        body, mesh=mesh, in_specs=placed, out_specs=P("wide", "narrow"), check_vma=False
    )
```

```python
import jax
import jax.numpy as jnp
from jax import lax
from jax.sharding import PartitionSpec as P

BO = 32
CHUNK = 256


def block_masks(size_pad, tensor_flags, occupied_flags, virtual_flags, atom_index):
    nearby_sizes = lax.dynamic_slice(size_pad, (atom_index,), (5,))
    present = (nearby_sizes > 0).astype(jnp.int32)
    orbital = jnp.arange(BO, dtype=jnp.int32)
    zero_index = jnp.zeros((), jnp.int32)
    row_flags = lax.dynamic_slice(tensor_flags, (atom_index + 1, zero_index), (3, 3))
    row_ok = (orbital[None, :] < nearby_sizes[1:4, None]).astype(jnp.int32)
    partner = jnp.stack([nearby_sizes[r : r + 3] for r in range(3)])
    column_ok = (orbital[None, None, :] < partner[:, :, None]).astype(jnp.int32)
    entry_mask = row_flags[:, :, None, None] * row_ok[:, None, :, None] * column_ok[:, :, None, :]
    tensor_mask = entry_mask.reshape(3, 3, 1, BO * BO).astype(jnp.bfloat16)
    occupied_mask = (
        lax.dynamic_slice(occupied_flags, (atom_index + 2, zero_index), (1, 3))[0] * present[1:4]
    )
    partner_present = jnp.stack([present[r : r + 3] for r in range(3)])
    virtual_mask = (
        lax.dynamic_slice(virtual_flags, (atom_index + 1, zero_index), (3, 3))
        * present[1:4, None]
        * partner_present
    )
    return (tensor_mask, occupied_mask.astype(jnp.bfloat16), virtual_mask.astype(jnp.bfloat16))


def left_kron(block, row_mask):
    size = BO * BO
    spread = jnp.repeat(block.T, BO, axis=1)
    full = jnp.broadcast_to(spread[:, None, :], (BO, BO, size)).reshape(size, size)
    rows = lax.broadcasted_iota(jnp.int32, (size, size), 0)
    columns = lax.broadcasted_iota(jnp.int32, (size, size), 1)
    keep = (rows % BO) == (columns % BO)
    return (jnp.where(keep, full, 0.0) * row_mask[:, None]).astype(jnp.bfloat16)


def right_kron(block, row_mask):
    size = BO * BO
    spread = jnp.tile(block, (1, BO))
    full = jnp.broadcast_to(spread[None, :, :], (BO, BO, size)).reshape(size, size)
    rows = lax.broadcasted_iota(jnp.int32, (size, size), 0)
    columns = lax.broadcasted_iota(jnp.int32, (size, size), 1)
    keep = (rows // BO) == (columns // BO)
    return (jnp.where(keep, full, 0.0) * row_mask[:, None]).astype(jnp.bfloat16)


def right_kron_chunks(block, row_mask, chunk):
    groups = chunk // BO
    spread = jnp.tile(block, (1, groups))
    full = jnp.broadcast_to(spread[None, :, :], (groups, BO, chunk)).reshape(chunk, chunk)
    rows = lax.broadcasted_iota(jnp.int32, (chunk, chunk), 0)
    columns = lax.broadcasted_iota(jnp.int32, (chunk, chunk), 1)
    keep = (rows // BO) == (columns // BO)
    sized = jnp.where(keep, full, 0.0)
    masks = row_mask.reshape(-1, chunk)
    return (sized[None] * masks[:, :, None]).astype(jnp.bfloat16)


def contract(rows, tensor_mask, occupied_row, virtual_rows):
    occupied_blocks = occupied_row.reshape(3, BO, BO).astype(jnp.float32)
    virtual_blocks = virtual_rows.reshape(3, 3, BO, BO).astype(jnp.float32)
    row_masks = tensor_mask.reshape(3, 3, BO * BO).astype(jnp.float32)
    occupied_terms = []
    virtual_terms = []
    for out_band in range(5):
        total_left = None
        total_right = None
        for left_band in range(3):
            right_band = out_band - left_band
            if 0 <= right_band < 3:
                left = jnp.dot(
                    rows[left_band][right_band],
                    left_kron(occupied_blocks[left_band], row_masks[left_band, right_band]),
                    preferred_element_type=jnp.float32,
                )
                source = rows[1][left_band]
                pieces = right_kron_chunks(virtual_blocks[left_band, right_band], row_masks[1, left_band], CHUNK)
                right = jnp.concatenate(
                    [
                        jnp.dot(
                            source[:, piece * CHUNK : (piece + 1) * CHUNK],
                            pieces[piece],
                            preferred_element_type=jnp.float32,
                        )
                        for piece in range(pieces.shape[0])
                    ],
                    1,
                )
                total_left = left if total_left is None else total_left + left
                total_right = right if total_right is None else total_right + right
        occupied_terms.append(total_left.astype(jnp.bfloat16))
        virtual_terms.append(total_right.astype(jnp.bfloat16))
    left_product = jnp.concatenate(occupied_terms, 1)
    right_product = jnp.concatenate(virtual_terms, 1)
    return (left_product, right_product)


def neighbours(array, axis):
    devices = lax.axis_size(axis)
    up = [(i, (i + 1) % devices) for i in range(devices - 1)]
    down = [(j, i) for i, j in up]
    before = lax.ppermute(array, axis, up)
    after = lax.ppermute(array, axis, down)
    return before, after


def body(tensor, occupied, virtual, atom_size, tensor_pattern, occupied_pattern, virtual_pattern):
    narrow_count = lax.axis_size("narrow")
    atom_index = lax.axis_index("wide") * narrow_count + lax.axis_index("narrow")
    own_bands = []
    before_bands = []
    after_bands = []
    for band in range(tensor.shape[1]):
        sectioned_rows = tensor[:, band][:, None]
        regrouped = lax.all_to_all(sectioned_rows, "narrow", split_axis=0, concat_axis=2, tiled=True)
        own_band = regrouped[0, 0]
        before_band, after_band = neighbours(own_band, ("wide", "narrow"))
        own_bands.append(own_band)
        before_bands.append(before_band)
        after_bands.append(after_band)
    own, before, after = (tuple(own_bands), tuple(before_bands), tuple(after_bands))
    occupied_pad = jnp.pad(occupied, ((1, 1), (0, 0), (0, 0)))
    virtual_pad = jnp.pad(virtual, ((1, 1), (0, 0), (0, 0)))
    size_pad = jnp.pad(atom_size, 2)
    tensor_flags = jnp.pad(tensor_pattern, ((2, 2), (0, 0)))
    occupied_flags = jnp.pad(occupied_pattern, ((2, 2), (0, 0)))
    virtual_flags = jnp.pad(virtual_pattern, ((2, 2), (0, 0)))
    tensor_mask, occupied_mask, virtual_mask = block_masks(
        size_pad, tensor_flags, occupied_flags, virtual_flags, atom_index
    )
    occupied_row = (
        lax.dynamic_slice_in_dim(occupied_pad, atom_index + 1, 1, 0)[0] * occupied_mask[:, None]
    )
    virtual_rows = (
        lax.dynamic_slice_in_dim(virtual_pad, atom_index, 3, 0) * virtual_mask[:, :, None]
    )
    left_product, right_product = contract(
        (before, own, after), tensor_mask, occupied_row, virtual_rows
    )
    partial_response = lax.dot_general(
        left_product, right_product, (((1,), (1,)), ((), ())), preferred_element_type=jnp.float32
    )
    column_share = lax.psum_scatter(partial_response, "narrow", scatter_dimension=1, tiled=True)
    wide_count = lax.axis_size("wide")
    row_pieces = column_share.reshape(wide_count, column_share.shape[0] // wide_count, column_share.shape[1])
    gathered = lax.all_to_all(row_pieces, "wide", 0, 0, tiled=True)
    return gathered.sum(0)


def solution(mesh):
    placed = (P("wide", None, "narrow", None), P(), P(), P(), P(), P(), P())
    return jax.shard_map(
        body, mesh=mesh, in_specs=placed, out_specs=P("wide", "narrow"), check_vma=False
    )
```

```python
import jax
import jax.numpy as jnp
from jax import lax
from jax.sharding import PartitionSpec as P

BO = 32
CHUNK = 256


def block_masks(size_pad, tensor_flags, occupied_flags, virtual_flags, atom_index):
    nearby_sizes = lax.dynamic_slice(size_pad, (atom_index,), (5,))
    present = (nearby_sizes > 0).astype(jnp.int32)
    orbital = jnp.arange(BO, dtype=jnp.int32)
    zero_index = jnp.zeros((), jnp.int32)
    row_flags = lax.dynamic_slice(tensor_flags, (atom_index + 1, zero_index), (3, 3))
    row_ok = (orbital[None, :] < nearby_sizes[1:4, None]).astype(jnp.int32)
    partner = jnp.stack([nearby_sizes[r : r + 3] for r in range(3)])
    column_ok = (orbital[None, None, :] < partner[:, :, None]).astype(jnp.int32)
    entry_mask = row_flags[:, :, None, None] * row_ok[:, None, :, None] * column_ok[:, :, None, :]
    tensor_mask = entry_mask.reshape(3, 3, 1, BO * BO).astype(jnp.bfloat16)
    occupied_mask = (
        lax.dynamic_slice(occupied_flags, (atom_index + 2, zero_index), (1, 3))[0] * present[1:4]
    )
    partner_present = jnp.stack([present[r : r + 3] for r in range(3)])
    virtual_mask = (
        lax.dynamic_slice(virtual_flags, (atom_index + 1, zero_index), (3, 3))
        * present[1:4, None]
        * partner_present
    )
    return (tensor_mask, occupied_mask.astype(jnp.bfloat16), virtual_mask.astype(jnp.bfloat16))


def left_kron(block, row_mask):
    size = BO * BO
    spread = jnp.repeat(block.T, BO, axis=1)
    full = jnp.broadcast_to(spread[:, None, :], (BO, BO, size)).reshape(size, size)
    rows = lax.broadcasted_iota(jnp.int32, (size, size), 0)
    columns = lax.broadcasted_iota(jnp.int32, (size, size), 1)
    keep = (rows % BO) == (columns % BO)
    return (jnp.where(keep, full, 0.0) * row_mask[:, None]).astype(jnp.bfloat16)


def right_kron(block, row_mask):
    size = BO * BO
    spread = jnp.tile(block, (1, BO))
    full = jnp.broadcast_to(spread[None, :, :], (BO, BO, size)).reshape(size, size)
    rows = lax.broadcasted_iota(jnp.int32, (size, size), 0)
    columns = lax.broadcasted_iota(jnp.int32, (size, size), 1)
    keep = (rows // BO) == (columns // BO)
    return (jnp.where(keep, full, 0.0) * row_mask[:, None]).astype(jnp.bfloat16)


def right_kron_chunks(block, row_mask, chunk):
    groups = chunk // BO
    spread = jnp.tile(block, (1, groups))
    full = jnp.broadcast_to(spread[None, :, :], (groups, BO, chunk)).reshape(chunk, chunk)
    rows = lax.broadcasted_iota(jnp.int32, (chunk, chunk), 0)
    columns = lax.broadcasted_iota(jnp.int32, (chunk, chunk), 1)
    keep = (rows // BO) == (columns // BO)
    sized = jnp.where(keep, full, 0.0)
    masks = row_mask.reshape(-1, chunk)
    return (sized[None] * masks[:, :, None]).astype(jnp.bfloat16)


def contract(rows, tensor_mask, occupied_row, virtual_rows):
    occupied_blocks = occupied_row.reshape(3, BO, BO).astype(jnp.float32)
    virtual_blocks = virtual_rows.reshape(3, 3, BO, BO).astype(jnp.float32)
    row_masks = tensor_mask.reshape(3, 3, BO * BO).astype(jnp.float32)
    occupied_terms = []
    virtual_terms = []
    for out_band in range(5):
        total_left = None
        total_right = None
        for left_band in range(3):
            right_band = out_band - left_band
            if 0 <= right_band < 3:
                left = jnp.dot(
                    rows[left_band][right_band],
                    left_kron(occupied_blocks[left_band], row_masks[left_band, right_band]),
                    preferred_element_type=jnp.float32,
                )
                source = rows[1][left_band]
                pieces = right_kron_chunks(virtual_blocks[left_band, right_band], row_masks[1, left_band], CHUNK)
                right = jnp.concatenate(
                    [
                        jnp.dot(
                            source[:, piece * CHUNK : (piece + 1) * CHUNK],
                            pieces[piece],
                            preferred_element_type=jnp.float32,
                        )
                        for piece in range(pieces.shape[0])
                    ],
                    1,
                )
                total_left = left if total_left is None else total_left + left
                total_right = right if total_right is None else total_right + right
        occupied_terms.append(total_left.astype(jnp.bfloat16))
        virtual_terms.append(total_right.astype(jnp.bfloat16))
    left_product = jnp.concatenate(occupied_terms, 1)
    right_product = jnp.concatenate(virtual_terms, 1)
    return (left_product, right_product)


def neighbours(array, axis):
    devices = lax.axis_size(axis)
    up = [(i, (i + 1) % devices) for i in range(devices - 1)]
    down = [(j, i) for i, j in up]
    before = lax.ppermute(array, axis, up)
    after = lax.ppermute(array, axis, down)
    return before, after


def body(tensor, occupied, virtual, atom_size, tensor_pattern, occupied_pattern, virtual_pattern):
    narrow_count = lax.axis_size("narrow")
    atom_index = lax.axis_index("wide") * narrow_count + lax.axis_index("narrow")
    sectioned_rows = tensor[:, None]
    regrouped = lax.all_to_all(sectioned_rows, "narrow", split_axis=0, concat_axis=3, tiled=True)
    own = regrouped[0, 0]
    before, after = neighbours(own, ("wide", "narrow"))
    occupied_pad = jnp.pad(occupied, ((1, 1), (0, 0), (0, 0)))
    virtual_pad = jnp.pad(virtual, ((1, 1), (0, 0), (0, 0)))
    size_pad = jnp.pad(atom_size, 2)
    tensor_flags = jnp.pad(tensor_pattern, ((2, 2), (0, 0)))
    occupied_flags = jnp.pad(occupied_pattern, ((2, 2), (0, 0)))
    virtual_flags = jnp.pad(virtual_pattern, ((2, 2), (0, 0)))
    tensor_mask, occupied_mask, virtual_mask = block_masks(
        size_pad, tensor_flags, occupied_flags, virtual_flags, atom_index
    )
    occupied_row = (
        lax.dynamic_slice_in_dim(occupied_pad, atom_index + 1, 1, 0)[0] * occupied_mask[:, None]
    )
    virtual_rows = (
        lax.dynamic_slice_in_dim(virtual_pad, atom_index, 3, 0) * virtual_mask[:, :, None]
    )
    left_product, right_product = contract(
        (before, own, after), tensor_mask, occupied_row, virtual_rows
    )
    partial_response = lax.dot_general(
        left_product, right_product, (((1,), (1,)), ((), ())), preferred_element_type=jnp.float32
    )
    wide_count = lax.axis_size("wide")
    rows, columns = partial_response.shape
    blocks = partial_response.reshape(wide_count, rows // wide_count, narrow_count, columns // narrow_count)
    blocks = blocks.transpose(0, 2, 1, 3).reshape(
        wide_count * narrow_count, rows // wide_count, columns // narrow_count
    )
    gathered = lax.all_to_all(blocks, ("wide", "narrow"), 0, 0, tiled=True)
    return gathered.sum(0)


def solution(mesh):
    placed = (P("wide", None, "narrow", None), P(), P(), P(), P(), P(), P())
    return jax.shard_map(
        body, mesh=mesh, in_specs=placed, out_specs=P("wide", "narrow"), check_vma=False
    )
```

```python
import jax
import jax.numpy as jnp
from jax import lax
from jax.sharding import PartitionSpec as P

BO = 32
CHUNK = 256


def block_masks(size_pad, tensor_flags, occupied_flags, virtual_flags, atom_index):
    nearby_sizes = lax.dynamic_slice(size_pad, (atom_index,), (5,))
    present = (nearby_sizes > 0).astype(jnp.int32)
    orbital = jnp.arange(BO, dtype=jnp.int32)
    zero_index = jnp.zeros((), jnp.int32)
    row_flags = lax.dynamic_slice(tensor_flags, (atom_index + 1, zero_index), (3, 3))
    row_ok = (orbital[None, :] < nearby_sizes[1:4, None]).astype(jnp.int32)
    partner = jnp.stack([nearby_sizes[r : r + 3] for r in range(3)])
    column_ok = (orbital[None, None, :] < partner[:, :, None]).astype(jnp.int32)
    entry_mask = row_flags[:, :, None, None] * row_ok[:, None, :, None] * column_ok[:, :, None, :]
    tensor_mask = entry_mask.reshape(3, 3, 1, BO * BO).astype(jnp.bfloat16)
    occupied_mask = (
        lax.dynamic_slice(occupied_flags, (atom_index + 2, zero_index), (1, 3))[0] * present[1:4]
    )
    partner_present = jnp.stack([present[r : r + 3] for r in range(3)])
    virtual_mask = (
        lax.dynamic_slice(virtual_flags, (atom_index + 1, zero_index), (3, 3))
        * present[1:4, None]
        * partner_present
    )
    return (tensor_mask, occupied_mask.astype(jnp.bfloat16), virtual_mask.astype(jnp.bfloat16))


def left_kron(block, row_mask):
    size = BO * BO
    spread = jnp.repeat(block.T, BO, axis=1)
    full = jnp.broadcast_to(spread[:, None, :], (BO, BO, size)).reshape(size, size)
    rows = lax.broadcasted_iota(jnp.int32, (size, size), 0)
    columns = lax.broadcasted_iota(jnp.int32, (size, size), 1)
    keep = (rows % BO) == (columns % BO)
    return (jnp.where(keep, full, 0.0) * row_mask[:, None]).astype(jnp.bfloat16)


def right_kron(block, row_mask):
    size = BO * BO
    spread = jnp.tile(block, (1, BO))
    full = jnp.broadcast_to(spread[None, :, :], (BO, BO, size)).reshape(size, size)
    rows = lax.broadcasted_iota(jnp.int32, (size, size), 0)
    columns = lax.broadcasted_iota(jnp.int32, (size, size), 1)
    keep = (rows // BO) == (columns // BO)
    return (jnp.where(keep, full, 0.0) * row_mask[:, None]).astype(jnp.bfloat16)


def right_kron_chunks(block, row_mask, chunk):
    groups = chunk // BO
    spread = jnp.tile(block, (1, groups))
    full = jnp.broadcast_to(spread[None, :, :], (groups, BO, chunk)).reshape(chunk, chunk)
    rows = lax.broadcasted_iota(jnp.int32, (chunk, chunk), 0)
    columns = lax.broadcasted_iota(jnp.int32, (chunk, chunk), 1)
    keep = (rows // BO) == (columns // BO)
    sized = jnp.where(keep, full, 0.0)
    masks = row_mask.reshape(-1, chunk)
    return (sized[None] * masks[:, :, None]).astype(jnp.bfloat16)


def contract(rows, tensor_mask, occupied_row, virtual_rows):
    occupied_blocks = occupied_row.reshape(3, BO, BO).astype(jnp.float32)
    virtual_blocks = virtual_rows.reshape(3, 3, BO, BO).astype(jnp.float32)
    row_masks = tensor_mask.reshape(3, 3, BO * BO).astype(jnp.float32)
    occupied_terms = []
    virtual_terms = []
    for out_band in range(5):
        total_left = None
        total_right = None
        for left_band in range(3):
            right_band = out_band - left_band
            if 0 <= right_band < 3:
                left = jnp.dot(
                    rows[left_band][right_band],
                    left_kron(occupied_blocks[left_band], row_masks[left_band, right_band]),
                    preferred_element_type=jnp.float32,
                )
                source = rows[1][left_band]
                pieces = right_kron_chunks(virtual_blocks[left_band, right_band], row_masks[1, left_band], CHUNK)
                right = jnp.concatenate(
                    [
                        jnp.dot(
                            source[:, piece * CHUNK : (piece + 1) * CHUNK],
                            pieces[piece],
                            preferred_element_type=jnp.float32,
                        )
                        for piece in range(pieces.shape[0])
                    ],
                    1,
                )
                total_left = left if total_left is None else total_left + left
                total_right = right if total_right is None else total_right + right
        occupied_terms.append(total_left.astype(jnp.bfloat16))
        virtual_terms.append(total_right.astype(jnp.bfloat16))
    left_product = jnp.concatenate(occupied_terms, 1)
    right_product = jnp.concatenate(virtual_terms, 1)
    return (left_product, right_product)


def neighbours(array, axis):
    devices = lax.axis_size(axis)
    up = [(i, (i + 1) % devices) for i in range(devices - 1)]
    down = [(j, i) for i, j in up]
    before = lax.ppermute(array, axis, up)
    after = lax.ppermute(array, axis, down)
    return before, after


def body(tensor, occupied, virtual, atom_size, tensor_pattern, occupied_pattern, virtual_pattern):
    narrow_count = lax.axis_size("narrow")
    atom_index = lax.axis_index("wide") * narrow_count + lax.axis_index("narrow")
    sectioned_rows = tensor[:, None]
    regrouped = lax.all_to_all(sectioned_rows, "narrow", split_axis=0, concat_axis=3, tiled=True)
    own = regrouped[0, 0]
    before, after = neighbours(own, ("wide", "narrow"))
    occupied_pad = jnp.pad(occupied, ((1, 1), (0, 0), (0, 0)))
    virtual_pad = jnp.pad(virtual, ((1, 1), (0, 0), (0, 0)))
    size_pad = jnp.pad(atom_size, 2)
    tensor_flags = jnp.pad(tensor_pattern, ((2, 2), (0, 0)))
    occupied_flags = jnp.pad(occupied_pattern, ((2, 2), (0, 0)))
    virtual_flags = jnp.pad(virtual_pattern, ((2, 2), (0, 0)))
    tensor_mask, occupied_mask, virtual_mask = block_masks(
        size_pad, tensor_flags, occupied_flags, virtual_flags, atom_index
    )
    occupied_row = (
        lax.dynamic_slice_in_dim(occupied_pad, atom_index + 1, 1, 0)[0] * occupied_mask[:, None]
    )
    virtual_rows = (
        lax.dynamic_slice_in_dim(virtual_pad, atom_index, 3, 0) * virtual_mask[:, :, None]
    )
    left_product, right_product = contract(
        (before, own, after), tensor_mask, occupied_row, virtual_rows
    )
    partial_response = lax.dot_general(
        left_product, right_product, (((1,), (1,)), ((), ())), preferred_element_type=jnp.float32
    )
    rows, columns = partial_response.shape
    column_blocks = partial_response.reshape(rows, narrow_count, columns // narrow_count).transpose(1, 0, 2)
    column_share = lax.psum_scatter(
        column_blocks.reshape(narrow_count * rows, columns // narrow_count), "narrow", scatter_dimension=0, tiled=True
    )
    wide_count = lax.axis_size("wide")
    row_pieces = column_share.reshape(wide_count, column_share.shape[0] // wide_count, column_share.shape[1])
    gathered = lax.all_to_all(row_pieces, "wide", 0, 0, tiled=True)
    return gathered.sum(0)


def solution(mesh):
    placed = (P("wide", None, "narrow", None), P(), P(), P(), P(), P(), P())
    return jax.shard_map(
        body, mesh=mesh, in_specs=placed, out_specs=P("wide", "narrow"), check_vma=False
    )
```

```python
import jax
import jax.numpy as jnp
from jax import lax
from jax.sharding import PartitionSpec as P

BO = 32
CHUNK = 512


def block_masks(size_pad, tensor_flags, occupied_flags, virtual_flags, atom_index):
    nearby_sizes = lax.dynamic_slice(size_pad, (atom_index,), (5,))
    present = (nearby_sizes > 0).astype(jnp.int32)
    orbital = jnp.arange(BO, dtype=jnp.int32)
    zero_index = jnp.zeros((), jnp.int32)
    row_flags = lax.dynamic_slice(tensor_flags, (atom_index + 1, zero_index), (3, 3))
    row_ok = (orbital[None, :] < nearby_sizes[1:4, None]).astype(jnp.int32)
    partner = jnp.stack([nearby_sizes[r : r + 3] for r in range(3)])
    column_ok = (orbital[None, None, :] < partner[:, :, None]).astype(jnp.int32)
    entry_mask = row_flags[:, :, None, None] * row_ok[:, None, :, None] * column_ok[:, :, None, :]
    tensor_mask = entry_mask.reshape(3, 3, 1, BO * BO).astype(jnp.bfloat16)
    occupied_mask = (
        lax.dynamic_slice(occupied_flags, (atom_index + 2, zero_index), (1, 3))[0] * present[1:4]
    )
    partner_present = jnp.stack([present[r : r + 3] for r in range(3)])
    virtual_mask = (
        lax.dynamic_slice(virtual_flags, (atom_index + 1, zero_index), (3, 3))
        * present[1:4, None]
        * partner_present
    )
    return (tensor_mask, occupied_mask.astype(jnp.bfloat16), virtual_mask.astype(jnp.bfloat16))


def left_kron(block, row_mask):
    size = BO * BO
    spread = jnp.repeat(block.T, BO, axis=1)
    full = jnp.broadcast_to(spread[:, None, :], (BO, BO, size)).reshape(size, size)
    rows = lax.broadcasted_iota(jnp.int32, (size, size), 0)
    columns = lax.broadcasted_iota(jnp.int32, (size, size), 1)
    keep = (rows % BO) == (columns % BO)
    return (jnp.where(keep, full, 0.0) * row_mask[:, None]).astype(jnp.bfloat16)


def right_kron(block, row_mask):
    size = BO * BO
    spread = jnp.tile(block, (1, BO))
    full = jnp.broadcast_to(spread[None, :, :], (BO, BO, size)).reshape(size, size)
    rows = lax.broadcasted_iota(jnp.int32, (size, size), 0)
    columns = lax.broadcasted_iota(jnp.int32, (size, size), 1)
    keep = (rows // BO) == (columns // BO)
    return (jnp.where(keep, full, 0.0) * row_mask[:, None]).astype(jnp.bfloat16)


def right_kron_chunks(block, row_mask, chunk):
    groups = chunk // BO
    spread = jnp.tile(block, (1, groups))
    full = jnp.broadcast_to(spread[None, :, :], (groups, BO, chunk)).reshape(chunk, chunk)
    rows = lax.broadcasted_iota(jnp.int32, (chunk, chunk), 0)
    columns = lax.broadcasted_iota(jnp.int32, (chunk, chunk), 1)
    keep = (rows // BO) == (columns // BO)
    sized = jnp.where(keep, full, 0.0)
    masks = row_mask.reshape(-1, chunk)
    return (sized[None] * masks[:, :, None]).astype(jnp.bfloat16)


def contract(rows, tensor_mask, occupied_row, virtual_rows):
    occupied_blocks = occupied_row.reshape(3, BO, BO).astype(jnp.float32)
    virtual_blocks = virtual_rows.reshape(3, 3, BO, BO).astype(jnp.float32)
    row_masks = tensor_mask.reshape(3, 3, BO * BO).astype(jnp.float32)
    occupied_terms = []
    virtual_terms = []
    for out_band in range(5):
        total_left = None
        total_right = None
        for left_band in range(3):
            right_band = out_band - left_band
            if 0 <= right_band < 3:
                left = jnp.dot(
                    rows[left_band][right_band],
                    left_kron(occupied_blocks[left_band], row_masks[left_band, right_band]),
                    preferred_element_type=jnp.float32,
                )
                source = rows[1][left_band]
                pieces = right_kron_chunks(virtual_blocks[left_band, right_band], row_masks[1, left_band], CHUNK)
                right = jnp.concatenate(
                    [
                        jnp.dot(
                            source[:, piece * CHUNK : (piece + 1) * CHUNK],
                            pieces[piece],
                            preferred_element_type=jnp.float32,
                        )
                        for piece in range(pieces.shape[0])
                    ],
                    1,
                )
                total_left = left if total_left is None else total_left + left
                total_right = right if total_right is None else total_right + right
        occupied_terms.append(total_left.astype(jnp.bfloat16))
        virtual_terms.append(total_right.astype(jnp.bfloat16))
    left_product = jnp.concatenate(occupied_terms, 1)
    right_product = jnp.concatenate(virtual_terms, 1)
    return (left_product, right_product)


def neighbours(array, axis):
    devices = lax.axis_size(axis)
    up = [(i, (i + 1) % devices) for i in range(devices - 1)]
    down = [(j, i) for i, j in up]
    before = lax.ppermute(array, axis, up)
    after = lax.ppermute(array, axis, down)
    return before, after


def body(tensor, occupied, virtual, atom_size, tensor_pattern, occupied_pattern, virtual_pattern):
    narrow_count = lax.axis_size("narrow")
    atom_index = lax.axis_index("wide") * narrow_count + lax.axis_index("narrow")
    sectioned_rows = tensor[:, None]
    regrouped = lax.all_to_all(sectioned_rows, "narrow", split_axis=0, concat_axis=3, tiled=True)
    own = regrouped[0, 0]
    before, after = neighbours(own, ("wide", "narrow"))
    occupied_pad = jnp.pad(occupied, ((1, 1), (0, 0), (0, 0)))
    virtual_pad = jnp.pad(virtual, ((1, 1), (0, 0), (0, 0)))
    size_pad = jnp.pad(atom_size, 2)
    tensor_flags = jnp.pad(tensor_pattern, ((2, 2), (0, 0)))
    occupied_flags = jnp.pad(occupied_pattern, ((2, 2), (0, 0)))
    virtual_flags = jnp.pad(virtual_pattern, ((2, 2), (0, 0)))
    tensor_mask, occupied_mask, virtual_mask = block_masks(
        size_pad, tensor_flags, occupied_flags, virtual_flags, atom_index
    )
    occupied_row = (
        lax.dynamic_slice_in_dim(occupied_pad, atom_index + 1, 1, 0)[0] * occupied_mask[:, None]
    )
    virtual_rows = (
        lax.dynamic_slice_in_dim(virtual_pad, atom_index, 3, 0) * virtual_mask[:, :, None]
    )
    left_product, right_product = contract(
        (before, own, after), tensor_mask, occupied_row, virtual_rows
    )
    partial_response = lax.dot_general(
        left_product, right_product, (((1,), (1,)), ((), ())), preferred_element_type=jnp.float32
    )
    column_share = lax.psum_scatter(partial_response, "narrow", scatter_dimension=1, tiled=True)
    wide_count = lax.axis_size("wide")
    row_pieces = column_share.reshape(wide_count, column_share.shape[0] // wide_count, column_share.shape[1])
    gathered = lax.all_to_all(row_pieces, "wide", 0, 0, tiled=True)
    return gathered.sum(0)


def solution(mesh):
    placed = (P("wide", None, "narrow", None), P(), P(), P(), P(), P(), P())
    return jax.shard_map(
        body, mesh=mesh, in_specs=placed, out_specs=P("wide", "narrow"), check_vma=False
    )
```
